1024 devices in a mesh: section: 2 (over z_hi), dp: 32 (over x, y), seq: 16 (over z_lo, core).
Axes of the slice: x: 4, y: 8, z: 16 (z_hi: 2, z_lo: 8; z = z_hi * 8 + z_lo), core: 2. Of those that a mesh axis runs over, the one named last changes fastest.
Arguments:
- saved_inputs: bfloat16 [2, 64, 2048, 768], P('section', 'dp', 'seq'), may hold values from -50 to 50
- pooled_adjoint: bfloat16 [64, 1024, 768], P('dp', 'seq'), may hold values from -6 to 6
- weights: bfloat16 [2, 768, 2304], P('section', 'dp'), may hold values from -0.125 to 0.125
Outputs:
- input_adjoint: bfloat16 [2, 64, 2048, 768], P('section', 'dp', 'seq')
- weight_grad: bfloat16 [2, 768, 2304], P('section', 'dp')
The draws below stay inside these ranges and needn't reach their ends.
All inputs are finite; a program needn't handle non-finite values.
Results may differ from the reference program's by a relative error of at most 0.023.
Values may be sent and summed in bfloat16 or wider, within the bound.
No kernel may reach another device: no remote copies, remote signals or barrier semaphores. Data moves between devices by JAX's collectives and lax.ppermute only.
A program may use at most 32 MiB of HBM per device.

```python
import math
import jax
import jax.numpy as jnp
from jax import lax

C = 768
ROWS = 128
MB = 2
DILATION_STEP = 16
BLOCKS = 2
SEQUENCE_SITES = 2048
HALF = 1024
BATCH = 64
N_SECTION = 2
N_DP = 32
N_SEQ = 16


def draw_saved_inputs(key, part):
    first, second, third = jax.random.split(key, 3)
    shape = (N_SECTION, BATCH, SEQUENCE_SITES, C)
    base = jax.random.truncated_normal(first, -4.0, 4.0, shape, jnp.float32)
    row_scale = jnp.exp(jax.random.uniform(second, (N_SECTION, BATCH, SEQUENCE_SITES, 1), jnp.float32, math.log(0.3), math.log(3.0)))
    col_scale = jnp.exp(jax.random.uniform(third, (N_SECTION, 1, 1, C), jnp.float32, math.log(0.4), math.log(4.0)))
    return (base * row_scale * col_scale).astype(jnp.bfloat16)


def block_scale(rng, dims, pieces, least, top_value):
    gain, own = 1.0, jax.random.fold_in(rng, 6)
    for dim, blocks in pieces:
        heights = jnp.exp(jax.random.uniform(jax.random.fold_in(own, dim), (blocks,), jnp.float32, least / len(pieces), top_value / len(pieces)))
        gain = gain * jnp.repeat(heights, dims[dim] // blocks).reshape([-1 if axis == dim else 1 for axis in range(len(dims))])
    return gain


def centred(own_key, extent, scale, limit, cuts=(), held_as=jnp.bfloat16):
    level = block_scale(own_key, extent, cuts, -0.22, 0.18) if cuts else 1.0
    entries = jax.random.normal(own_key, extent, jnp.float32) * scale * level
    return jnp.minimum(jnp.maximum(entries, -limit), limit).astype(held_as)


def setup_inputs(seed: int = 0) -> dict:
    splits = jax.random.split(jax.random.key(seed), 4)
    return {
        "saved_inputs": draw_saved_inputs(jax.random.fold_in(splits[3], 71), 0),
        "pooled_adjoint": centred(splits[1], (BATCH, HALF, C), 1.0, 6.0, ((0, 32), (1, 16))),
        "weights": centred(splits[2], (BLOCKS, C, 3 * C), (3 * C) ** -0.5, 0.125, ((0, 2), (1, 32))),
    }


def gelu_gate(value):
    inner = 0.7978845608 * (value + 0.044715 * value * value * value)
    return 0.5 * value * (1.0 + jnp.tanh(inner))

def gelu_derivative(value):
    inner = 0.7978845608 * (value + 0.044715 * value * value * value)
    tangent = jnp.tanh(inner)
    return 0.5 * (1.0 + tangent) + 0.5 * value * (1.0 - tangent * tangent) * 0.7978845608 * (1.0 + 0.134145 * value * value)

def one_sequence(inputs, cotangent_state, kernel):
    value_rows = inputs.astype(jnp.float32)
    norm_scale = lax.rsqrt(lax.optimization_barrier(jnp.mean(value_rows * value_rows, axis=-1, keepdims=True)) + 1e-05)
    normalized_input = value_rows * norm_scale
    layer_activation = gelu_gate(normalized_input).astype(jnp.bfloat16)
    cotangent_padded = jnp.pad(cotangent_state, ((DILATION_STEP, DILATION_STEP), (0, 0)))
    activation_padded = jnp.pad(layer_activation, ((DILATION_STEP, DILATION_STEP), (0, 0)))
    cotangent_kernel_taps = jnp.concatenate([cotangent_padded[(2 - kernel_offset) * DILATION_STEP:(2 - kernel_offset) * DILATION_STEP + SEQUENCE_SITES] for kernel_offset in range(3)], axis=-1)
    reverse_propagate = jnp.dot(cotangent_kernel_taps, kernel.T, preferred_element_type=jnp.float32)
    derivative_gradient = reverse_propagate * gelu_derivative(normalized_input)
    centered_average = lax.optimization_barrier(jnp.mean(derivative_gradient * normalized_input, axis=-1, keepdims=True))
    block_output = (cotangent_state.astype(jnp.float32) + norm_scale * (derivative_gradient - normalized_input * centered_average)).astype(jnp.bfloat16)
    activation_kernel_taps = jnp.stack([activation_padded[kernel_offset * DILATION_STEP:kernel_offset * DILATION_STEP + SEQUENCE_SITES] for kernel_offset in range(3)], axis=0)
    activation_kernel_taps = activation_kernel_taps.astype(jnp.float32).reshape(3, N_SEQ, ROWS, C)
    adj_rows = cotangent_state.astype(jnp.float32).reshape(N_SEQ, ROWS, C)
    shard_terms = jnp.einsum('kjpc,jpo->jcko', activation_kernel_taps, adj_rows).reshape(N_SEQ, C, 3 * C)
    return (block_output, shard_terms)

def block_backward(inputs, cotangent_state, kernel):
    member_inputs = inputs.reshape(N_DP, MB, SEQUENCE_SITES, C)
    member_adjoint = cotangent_state.reshape(N_DP, MB, SEQUENCE_SITES, C)

    def one_member(pair):
        first, second = pair
        results = []
        partial_value = jnp.zeros((N_SEQ, C, 3 * C), jnp.float32)
        for micro_batch in range(MB):
            block_output, shard_terms = one_sequence(first[micro_batch], second[micro_batch], kernel)
            results.append(block_output)
            partial_value = partial_value + shard_terms
        rounded = partial_value.astype(jnp.bfloat16).astype(jnp.float32)
        return (jnp.stack(results, axis=0), lax.optimization_barrier(jnp.sum(rounded, axis=0)))
    results, partials = lax.map(one_member, (member_inputs, member_adjoint))
    grads = (lax.optimization_barrier(jnp.sum(partials, axis=0)) / BATCH).astype(jnp.bfloat16)
    return (results.reshape(BATCH, SEQUENCE_SITES, C), grads)

def reference(saved_inputs, pooled_adjoint, weights):
    upper_adjoint = jnp.repeat(pooled_adjoint, 2, axis=1) * 0.5
    upper_result, upper_grad = block_backward(saved_inputs[1], upper_adjoint, weights[1])
    lower_result, lower_grad = block_backward(saved_inputs[0], upper_result, weights[0])
    return (jnp.stack([lower_result, upper_result], axis=0), jnp.stack([lower_grad, upper_grad], axis=0))
```

```python
import jax
import jax.numpy as jnp
from jax import lax
from jax.sharding import PartitionSpec as P

DILATION_STEP = 16


def with_halo(array, sides, width):
    for axis, dim in sides:
        count, length = (lax.axis_size(axis), array.shape[dim])
        up = [(i, (i + 1) % count) for i in range(count - 1)]
        down = [(j, i) for i, j in up]
        last = lax.slice_in_dim(array, length - width, length, axis=dim)
        initial = lax.slice_in_dim(array, 0, width, axis=dim)
        before = lax.ppermute(last, axis, up)
        after = lax.ppermute(initial, axis, down)
        array = jnp.concatenate([before, array, after], axis=dim)
    return array


def from_behind(value, axis, steps):
    count = lax.axis_size(axis)
    initial, last = (max(0, -steps), min(count, count - steps))
    return lax.ppermute(value, axis, [(source, source + steps) for source in range(initial, last)])


def gelu_gate(value):
    inner = 0.7978845608 * (value + 0.044715 * value * value * value)
    return 0.5 * value * (1.0 + jnp.tanh(inner))


def gelu_derivative(value):
    inner = 0.7978845608 * (value + 0.044715 * value * value * value)
    tangent = jnp.tanh(inner)
    return 0.5 * (1.0 + tangent) + 0.5 * value * (1.0 - tangent * tangent) * 0.7978845608 * (
        1.0 + 0.134145 * value * value
    )


def select_position(array, position_index):
    return lax.dynamic_index_in_dim(array, position_index, 0, keepdims=False)


def local(saved_inputs, pooled_adjoint, weights):
    section_id = lax.axis_index("section")
    is_last = section_id == lax.axis_size("section") - 1
    micro_batch = saved_inputs.shape[1]
    batch_rows = saved_inputs.shape[2]
    channel_width = weights.shape[2] // 3
    dilation_amount = DILATION_STEP
    full_kernel = lax.all_gather(weights[0], "dp", axis=0, tiled=True)
    value_rows = saved_inputs[0].astype(jnp.float32)
    norm_scale = lax.rsqrt(jnp.mean(value_rows * value_rows, axis=-1, keepdims=True) + 1e-05)
    normalized_input = value_rows * norm_scale
    layer_activation = gelu_gate(normalized_input).astype(jnp.bfloat16)
    activation_widened_full = jnp.zeros(
        (micro_batch, batch_rows + 2 * dilation_amount, channel_width), jnp.bfloat16
    )
    grad_total = jnp.zeros((channel_width, 3 * channel_width), jnp.float32)
    results = jnp.zeros((micro_batch, batch_rows, channel_width), jnp.bfloat16)
    incoming = jnp.zeros((batch_rows, channel_width), jnp.bfloat16)
    for step_index in range(micro_batch + 1):
        slot_raw = step_index - 1 + section_id
        is_valid = (slot_raw >= 0) & (slot_raw < micro_batch)
        position_index = jnp.clip(slot_raw, 0, micro_batch - 1)
        upsampled = jnp.repeat(select_position(pooled_adjoint, position_index), 2, axis=0) * 0.5
        cotangent_state = jnp.where(is_last, upsampled, incoming)
        stacked_rows = jnp.stack(
            [select_position(layer_activation, position_index), cotangent_state], axis=0
        )
        paired_widened = with_halo(stacked_rows, (("seq", 1),), dilation_amount)
        activation_widened = paired_widened[0]
        cotangent_widened = paired_widened[1]
        current_act = select_position(activation_widened_full, position_index)
        activation_widened_full = lax.dynamic_update_index_in_dim(
            activation_widened_full,
            jnp.where(is_valid, activation_widened, current_act),
            position_index,
            0,
        )
        cotangent_kernel_taps = jnp.concatenate(
            [
                cotangent_widened[
                    (2 - kernel_offset) * dilation_amount : (2 - kernel_offset) * dilation_amount
                    + batch_rows
                ]
                for kernel_offset in range(3)
            ],
            axis=-1,
        )
        reverse_propagate = jnp.einsum(
            "pj,cj->pc", cotangent_kernel_taps, full_kernel, preferred_element_type=jnp.float32
        )
        position_normalized = select_position(normalized_input, position_index)
        position_scale = select_position(norm_scale, position_index)
        derivative_gradient = reverse_propagate * gelu_derivative(position_normalized)
        centered_average = jnp.mean(
            derivative_gradient * position_normalized, axis=-1, keepdims=True
        )
        block_output = (
            cotangent_state.astype(jnp.float32)
            + position_scale * (derivative_gradient - position_normalized * centered_average)
        ).astype(jnp.bfloat16)
        current = select_position(results, position_index)
        results = lax.dynamic_update_index_in_dim(
            results, jnp.where(is_valid, block_output, current), position_index, 0
        )
        activation_kernel_taps = jnp.stack(
            [
                activation_widened[
                    kernel_offset * dilation_amount : kernel_offset * dilation_amount + batch_rows
                ]
                for kernel_offset in range(3)
            ],
            axis=0,
        )
        grad_term = jnp.einsum(
            "kpc,po->cko",
            activation_kernel_taps,
            cotangent_state,
            preferred_element_type=jnp.float32,
        )
        grad_total = grad_total + jnp.where(
            is_valid, grad_term.reshape(channel_width, 3 * channel_width), 0.0
        )
        if step_index < micro_batch:
            incoming = from_behind(block_output, "section", -1)
    n_dp = lax.axis_size("dp")
    n_seq = lax.axis_size("seq")
    owned_rows = channel_width // n_dp
    pieces = grad_total.astype(jnp.bfloat16).reshape(n_dp, owned_rows, 3 * channel_width)
    received = lax.all_to_all(pieces, "dp", 0, 0, tiled=True)
    owned = jnp.sum(received.astype(jnp.float32), axis=0)
    column_chunk = 3 * channel_width // n_seq
    owned = owned.reshape(owned_rows, n_seq, column_chunk).transpose(1, 0, 2)
    gathered = lax.all_to_all(owned, "seq", 0, 0, tiled=True)
    summed = jnp.sum(gathered, axis=0)
    chunk_grad = (summed / (micro_batch * n_dp)).astype(jnp.bfloat16)
    weight_grad = lax.all_gather(chunk_grad, "seq", axis=1, tiled=True)
    return (results[None], weight_grad[None])


def solution(mesh):
    in_specs = (P("section", "dp", "seq", None), P("dp", "seq", None), P("section", "dp", None))
    out_specs = (P("section", "dp", "seq", None), P("section", "dp", None))
    return jax.shard_map(local, mesh=mesh, in_specs=in_specs, out_specs=out_specs, check_vma=False)
```

```python
import jax
import jax.numpy as jnp
from jax import lax
from jax.sharding import PartitionSpec as P

DILATION_STEP = 16


def with_halo(array, sides, width):
    for axis, dim in sides:
        count, length = (lax.axis_size(axis), array.shape[dim])
        up = [(i, (i + 1) % count) for i in range(count - 1)]
        down = [(j, i) for i, j in up]
        last = lax.slice_in_dim(array, length - width, length, axis=dim)
        initial = lax.slice_in_dim(array, 0, width, axis=dim)
        before = lax.ppermute(last, axis, up)
        after = lax.ppermute(initial, axis, down)
        array = jnp.concatenate([before, array, after], axis=dim)
    return array


def from_behind(value, axis, steps):
    count = lax.axis_size(axis)
    initial, last = (max(0, -steps), min(count, count - steps))
    return lax.ppermute(value, axis, [(source, source + steps) for source in range(initial, last)])


def gelu_gate(value):
    inner = 0.7978845608 * (value + 0.044715 * value * value * value)
    return 0.5 * value * (1.0 + jnp.tanh(inner))


def gelu_derivative(value):
    inner = 0.7978845608 * (value + 0.044715 * value * value * value)
    tangent = jnp.tanh(inner)
    return 0.5 * (1.0 + tangent) + 0.5 * value * (1.0 - tangent * tangent) * 0.7978845608 * (
        1.0 + 0.134145 * value * value
    )


def select_position(array, position_index):
    return lax.dynamic_index_in_dim(array, position_index, 0, keepdims=False)


def local(saved_inputs, pooled_adjoint, weights):
    section_id = lax.axis_index("section")
    is_last = section_id == lax.axis_size("section") - 1
    micro_batch = saved_inputs.shape[1]
    batch_rows = saved_inputs.shape[2]
    channel_width = weights.shape[2] // 3
    dilation_amount = DILATION_STEP
    seq_count = lax.axis_size("seq")
    core_index = lax.axis_index("seq") % 2
    half_columns = weights.shape[2] // 2
    own_half = lax.dynamic_slice_in_dim(weights[0], core_index * half_columns, half_columns, axis=1)
    gathered_half = lax.all_gather(own_half, "dp", axis=0, tiled=True)
    partner_half = lax.ppermute(gathered_half, "seq", [(j, j ^ 1) for j in range(seq_count)])
    full_kernel = jnp.where(
        core_index == 0,
        jnp.concatenate([gathered_half, partner_half], axis=1),
        jnp.concatenate([partner_half, gathered_half], axis=1),
    )
    value_rows = saved_inputs[0].astype(jnp.float32)
    norm_scale = lax.rsqrt(jnp.mean(value_rows * value_rows, axis=-1, keepdims=True) + 1e-05)
    normalized_input = value_rows * norm_scale
    layer_activation = gelu_gate(normalized_input).astype(jnp.bfloat16)
    activation_widened_full = jnp.zeros(
        (micro_batch, batch_rows + 2 * dilation_amount, channel_width), jnp.bfloat16
    )
    grad_total = jnp.zeros((channel_width, 3 * channel_width), jnp.float32)
    results = jnp.zeros((micro_batch, batch_rows, channel_width), jnp.bfloat16)
    incoming = jnp.zeros((batch_rows, channel_width), jnp.bfloat16)
    for step_index in range(micro_batch + 1):
        slot_raw = step_index - 1 + section_id
        is_valid = (slot_raw >= 0) & (slot_raw < micro_batch)
        position_index = jnp.clip(slot_raw, 0, micro_batch - 1)
        upsampled = jnp.repeat(select_position(pooled_adjoint, position_index), 2, axis=0) * 0.5
        cotangent_state = jnp.where(is_last, upsampled, incoming)
        stacked_rows = jnp.stack(
            [select_position(layer_activation, position_index), cotangent_state], axis=0
        )
        paired_widened = with_halo(stacked_rows, (("seq", 1),), dilation_amount)
        activation_widened = paired_widened[0]
        cotangent_widened = paired_widened[1]
        current_act = select_position(activation_widened_full, position_index)
        activation_widened_full = lax.dynamic_update_index_in_dim(
            activation_widened_full,
            jnp.where(is_valid, activation_widened, current_act),
            position_index,
            0,
        )
        cotangent_kernel_taps = jnp.concatenate(
            [
                cotangent_widened[
                    (2 - kernel_offset) * dilation_amount : (2 - kernel_offset) * dilation_amount
                    + batch_rows
                ]
                for kernel_offset in range(3)
            ],
            axis=-1,
        )
        reverse_propagate = jnp.einsum(
            "pj,cj->pc", cotangent_kernel_taps, full_kernel, preferred_element_type=jnp.float32
        )
        position_normalized = select_position(normalized_input, position_index)
        position_scale = select_position(norm_scale, position_index)
        derivative_gradient = reverse_propagate * gelu_derivative(position_normalized)
        centered_average = jnp.mean(
            derivative_gradient * position_normalized, axis=-1, keepdims=True
        )
        block_output = (
            cotangent_state.astype(jnp.float32)
            + position_scale * (derivative_gradient - position_normalized * centered_average)
        ).astype(jnp.bfloat16)
        current = select_position(results, position_index)
        results = lax.dynamic_update_index_in_dim(
            results, jnp.where(is_valid, block_output, current), position_index, 0
        )
        activation_kernel_taps = jnp.stack(
            [
                activation_widened[
                    kernel_offset * dilation_amount : kernel_offset * dilation_amount + batch_rows
                ]
                for kernel_offset in range(3)
            ],
            axis=0,
        )
        grad_term = jnp.einsum(
            "kpc,po->cko",
            activation_kernel_taps,
            cotangent_state,
            preferred_element_type=jnp.float32,
        )
        grad_total = grad_total + jnp.where(
            is_valid, grad_term.reshape(channel_width, 3 * channel_width), 0.0
        )
        if step_index < micro_batch:
            incoming = from_behind(block_output, "section", -1)
    n_dp = lax.axis_size("dp")
    n_seq = lax.axis_size("seq")
    owned_rows = channel_width // n_dp
    pieces = grad_total.astype(jnp.bfloat16).reshape(n_dp, owned_rows, 3 * channel_width)
    received = lax.all_to_all(pieces, "dp", 0, 0, tiled=True)
    owned = jnp.sum(received.astype(jnp.float32), axis=0)
    column_chunk = 3 * channel_width // n_seq
    owned = owned.reshape(owned_rows, n_seq, column_chunk).transpose(1, 0, 2)
    gathered = lax.all_to_all(owned, "seq", 0, 0, tiled=True)
    summed = jnp.sum(gathered, axis=0)
    chunk_grad = (summed / (micro_batch * n_dp)).astype(jnp.bfloat16)
    weight_grad = lax.all_gather(chunk_grad, "seq", axis=1, tiled=True)
    return (results[None], weight_grad[None])


def solution(mesh):
    in_specs = (P("section", "dp", "seq", None), P("dp", "seq", None), P("section", "dp", None))
    out_specs = (P("section", "dp", "seq", None), P("section", "dp", None))
    return jax.shard_map(local, mesh=mesh, in_specs=in_specs, out_specs=out_specs, check_vma=False)
```

```python
import jax
import jax.numpy as jnp
from jax import lax
from jax.sharding import Mesh, PartitionSpec as P

DILATION_STEP = 16
SEQ_AXES = ("zl", "core")


def with_halo(array, sides, width):
    for axis, dim in sides:
        count, length = (lax.axis_size(axis), array.shape[dim])
        up = [(i, (i + 1) % count) for i in range(count - 1)]
        down = [(j, i) for i, j in up]
        last = lax.slice_in_dim(array, length - width, length, axis=dim)
        initial = lax.slice_in_dim(array, 0, width, axis=dim)
        before = lax.ppermute(last, axis, up)
        after = lax.ppermute(initial, axis, down)
        array = jnp.concatenate([before, array, after], axis=dim)
    return array


def from_behind(value, axis, steps):
    count = lax.axis_size(axis)
    initial, last = (max(0, -steps), min(count, count - steps))
    return lax.ppermute(value, axis, [(source, source + steps) for source in range(initial, last)])


def gelu_gate(value):
    inner = 0.7978845608 * (value + 0.044715 * value * value * value)
    return 0.5 * value * (1.0 + jnp.tanh(inner))


def gelu_derivative(value):
    inner = 0.7978845608 * (value + 0.044715 * value * value * value)
    tangent = jnp.tanh(inner)
    return 0.5 * (1.0 + tangent) + 0.5 * value * (1.0 - tangent * tangent) * 0.7978845608 * (
        1.0 + 0.134145 * value * value
    )


def select_position(array, position_index):
    return lax.dynamic_index_in_dim(array, position_index, 0, keepdims=False)


def local(saved_inputs, pooled_adjoint, weights):
    section_id = lax.axis_index("section")
    is_last = section_id == lax.axis_size("section") - 1
    micro_batch = saved_inputs.shape[1]
    batch_rows = saved_inputs.shape[2]
    channel_width = weights.shape[2] // 3
    dilation_amount = DILATION_STEP
    full_kernel = lax.all_gather(weights[0], "y", axis=0, tiled=True)
    full_kernel = lax.all_gather(full_kernel, "x", axis=0, tiled=True)
    value_rows = saved_inputs[0].astype(jnp.float32)
    norm_scale = lax.rsqrt(jnp.mean(value_rows * value_rows, axis=-1, keepdims=True) + 1e-05)
    normalized_input = value_rows * norm_scale
    layer_activation = gelu_gate(normalized_input).astype(jnp.bfloat16)
    activation_widened_full = jnp.zeros(
        (micro_batch, batch_rows + 2 * dilation_amount, channel_width), jnp.bfloat16
    )
    grad_total = jnp.zeros((channel_width, 3 * channel_width), jnp.float32)
    results = jnp.zeros((micro_batch, batch_rows, channel_width), jnp.bfloat16)
    incoming = jnp.zeros((batch_rows, channel_width), jnp.bfloat16)
    for step_index in range(micro_batch + 1):
        slot_raw = step_index - 1 + section_id
        is_valid = (slot_raw >= 0) & (slot_raw < micro_batch)
        position_index = jnp.clip(slot_raw, 0, micro_batch - 1)
        upsampled = jnp.repeat(select_position(pooled_adjoint, position_index), 2, axis=0) * 0.5
        cotangent_state = jnp.where(is_last, upsampled, incoming)
        stacked_rows = jnp.stack(
            [select_position(layer_activation, position_index), cotangent_state], axis=0
        )
        paired_widened = with_halo(stacked_rows, ((SEQ_AXES, 1),), dilation_amount)
        activation_widened = paired_widened[0]
        cotangent_widened = paired_widened[1]
        current_act = select_position(activation_widened_full, position_index)
        activation_widened_full = lax.dynamic_update_index_in_dim(
            activation_widened_full,
            jnp.where(is_valid, activation_widened, current_act),
            position_index,
            0,
        )
        cotangent_kernel_taps = jnp.concatenate(
            [
                cotangent_widened[
                    (2 - kernel_offset) * dilation_amount : (2 - kernel_offset) * dilation_amount
                    + batch_rows
                ]
                for kernel_offset in range(3)
            ],
            axis=-1,
        )
        reverse_propagate = jnp.einsum(
            "pj,cj->pc", cotangent_kernel_taps, full_kernel, preferred_element_type=jnp.float32
        )
        position_normalized = select_position(normalized_input, position_index)
        position_scale = select_position(norm_scale, position_index)
        derivative_gradient = reverse_propagate * gelu_derivative(position_normalized)
        centered_average = jnp.mean(
            derivative_gradient * position_normalized, axis=-1, keepdims=True
        )
        block_output = (
            cotangent_state.astype(jnp.float32)
            + position_scale * (derivative_gradient - position_normalized * centered_average)
        ).astype(jnp.bfloat16)
        current = select_position(results, position_index)
        results = lax.dynamic_update_index_in_dim(
            results, jnp.where(is_valid, block_output, current), position_index, 0
        )
        activation_kernel_taps = jnp.stack(
            [
                activation_widened[
                    kernel_offset * dilation_amount : kernel_offset * dilation_amount + batch_rows
                ]
                for kernel_offset in range(3)
            ],
            axis=0,
        )
        grad_term = jnp.einsum(
            "kpc,po->cko",
            activation_kernel_taps,
            cotangent_state,
            preferred_element_type=jnp.float32,
        )
        grad_total = grad_total + jnp.where(
            is_valid, grad_term.reshape(channel_width, 3 * channel_width), 0.0
        )
        if step_index < micro_batch:
            incoming = from_behind(block_output, "section", -1)
    n_x = lax.axis_size("x")
    n_y = lax.axis_size("y")
    n_zl = lax.axis_size("zl")
    n_core = lax.axis_size("core")
    owned_rows = channel_width // (n_x * n_y)
    columns = 3 * channel_width
    pieces = grad_total.astype(jnp.bfloat16).reshape(n_x, n_y * owned_rows, columns)
    received = lax.all_to_all(pieces, "x", 0, 0, tiled=True)
    row_group = jnp.sum(received.astype(jnp.float32), axis=0).reshape(n_y, owned_rows, columns)
    received = lax.all_to_all(row_group, "y", 0, 0, tiled=True)
    owned = jnp.sum(received, axis=0)
    half = columns // n_core
    owned = owned.reshape(owned_rows, n_core, half).transpose(1, 0, 2)
    owned = jnp.sum(lax.all_to_all(owned, "core", 0, 0, tiled=True), axis=0)
    chunk = half // n_zl
    owned = owned.reshape(owned_rows, n_zl, chunk).transpose(1, 0, 2)
    summed = jnp.sum(lax.all_to_all(owned, "zl", 0, 0, tiled=True), axis=0)
    chunk_grad = (summed / (micro_batch * n_x * n_y)).astype(jnp.bfloat16)
    weight_grad = lax.all_gather(chunk_grad, "zl", axis=1, tiled=True)
    weight_grad = lax.all_gather(weight_grad, "core", axis=1, tiled=True)
    return (results[None], weight_grad[None])


def split_mesh(mesh):
    dp_devices = mesh.devices[0, :, 0]
    n_x = len({device.coords[0] for device in dp_devices})
    n_core = len({device.core_on_chip for device in mesh.devices[0, 0, :]})
    n_section, n_dp, n_seq = mesh.devices.shape
    shape = (n_section, n_x, n_dp // n_x, n_seq // n_core, n_core)
    return Mesh(mesh.devices.reshape(shape), ("section", "x", "y", "zl", "core"))


def solution(mesh):
    fine = split_mesh(mesh)
    dp, seq = ("x", "y"), SEQ_AXES
    in_specs = (P("section", dp, seq, None), P(dp, seq, None), P("section", dp, None))
    out_specs = (P("section", dp, seq, None), P("section", dp, None))
    return jax.shard_map(local, mesh=fine, in_specs=in_specs, out_specs=out_specs, check_vma=False)
```

```python
import jax
import jax.numpy as jnp
from jax import lax
from jax.sharding import Mesh, PartitionSpec as P

DILATION_STEP = 16
SEQ_AXES = ("zl", "core")


def with_halo(array, sides, width):
    for axis, dim in sides:
        count, length = (lax.axis_size(axis), array.shape[dim])
        up = [(i, (i + 1) % count) for i in range(count - 1)]
        down = [(j, i) for i, j in up]
        last = lax.slice_in_dim(array, length - width, length, axis=dim)
        initial = lax.slice_in_dim(array, 0, width, axis=dim)
        before = lax.ppermute(last, axis, up)
        after = lax.ppermute(initial, axis, down)
        array = jnp.concatenate([before, array, after], axis=dim)
    return array


def from_behind(value, axis, steps):
    count = lax.axis_size(axis)
    initial, last = (max(0, -steps), min(count, count - steps))
    return lax.ppermute(value, axis, [(source, source + steps) for source in range(initial, last)])


def gelu_gate(value):
    inner = 0.7978845608 * (value + 0.044715 * value * value * value)
    return 0.5 * value * (1.0 + jnp.tanh(inner))


def gelu_derivative(value):
    inner = 0.7978845608 * (value + 0.044715 * value * value * value)
    tangent = jnp.tanh(inner)
    return 0.5 * (1.0 + tangent) + 0.5 * value * (1.0 - tangent * tangent) * 0.7978845608 * (
        1.0 + 0.134145 * value * value
    )


def select_position(array, position_index):
    return lax.dynamic_index_in_dim(array, position_index, 0, keepdims=False)


def local(saved_inputs, pooled_adjoint, weights):
    section_id = lax.axis_index("section")
    is_last = section_id == lax.axis_size("section") - 1
    batch_rows = saved_inputs.shape[2]
    channel_width = weights.shape[2] // 3
    dilation_amount = DILATION_STEP
    full_kernel = lax.all_gather(weights[0], "y", axis=0, tiled=True)
    full_kernel = lax.all_gather(full_kernel, "x", axis=0, tiled=True)
    value_rows = saved_inputs[0].astype(jnp.float32)
    norm_scale = lax.rsqrt(jnp.mean(value_rows * value_rows, axis=-1, keepdims=True) + 1e-05)
    normalized_input = value_rows * norm_scale
    layer_activation = gelu_gate(normalized_input).astype(jnp.bfloat16)
    slope = gelu_derivative(normalized_input)
    upsampled = jnp.repeat(pooled_adjoint, 2, axis=1) * 0.5
    activation_widened = with_halo(layer_activation, ((SEQ_AXES, 1),), dilation_amount)

    def block(cotangent_state):
        cotangent_widened = with_halo(cotangent_state, ((SEQ_AXES, 1),), dilation_amount)
        cotangent_kernel_taps = jnp.concatenate(
            [
                cotangent_widened[
                    :,
                    (2 - kernel_offset) * dilation_amount : (2 - kernel_offset) * dilation_amount
                    + batch_rows,
                ]
                for kernel_offset in range(3)
            ],
            axis=-1,
        )
        reverse_propagate = jnp.einsum(
            "npj,cj->npc", cotangent_kernel_taps, full_kernel, preferred_element_type=jnp.float32
        )
        derivative_gradient = reverse_propagate * slope
        centered_average = jnp.mean(derivative_gradient * normalized_input, axis=-1, keepdims=True)
        return (
            cotangent_state.astype(jnp.float32)
            + norm_scale * (derivative_gradient - normalized_input * centered_average)
        ).astype(jnp.bfloat16)

    upper_output = block(upsampled)
    incoming = from_behind(upper_output, "section", -1)
    cotangent_state = jnp.where(is_last, upsampled, incoming)
    results = block(cotangent_state)
    activation_kernel_taps = jnp.stack(
        [
            activation_widened[
                :, kernel_offset * dilation_amount : kernel_offset * dilation_amount + batch_rows
            ]
            for kernel_offset in range(3)
        ],
        axis=0,
    )
    grad_total = jnp.einsum(
        "knpc,npo->cko", activation_kernel_taps, cotangent_state, preferred_element_type=jnp.float32
    ).reshape(channel_width, 3 * channel_width)
    micro_batch = saved_inputs.shape[1]
    n_dp = lax.axis_size(("x", "y"))
    n_seq = lax.axis_size(SEQ_AXES)
    owned_rows = channel_width // n_dp
    pieces = grad_total.astype(jnp.bfloat16).reshape(n_dp, owned_rows, 3 * channel_width)
    received = lax.all_to_all(pieces, ("x", "y"), 0, 0, tiled=True)
    owned = jnp.sum(received.astype(jnp.float32), axis=0)
    column_chunk = 3 * channel_width // n_seq
    owned = owned.reshape(owned_rows, n_seq, column_chunk).transpose(1, 0, 2)
    gathered = lax.all_to_all(owned, SEQ_AXES, 0, 0, tiled=True)
    summed = jnp.sum(gathered, axis=0)
    chunk_grad = (summed / (micro_batch * n_dp)).astype(jnp.bfloat16)
    weight_grad = lax.all_gather(chunk_grad, SEQ_AXES, axis=1, tiled=True)
    return (results[None], weight_grad[None])


def split_mesh(mesh):
    dp_devices = mesh.devices[0, :, 0]
    n_x = len({device.coords[0] for device in dp_devices})
    n_core = len({device.core_on_chip for device in mesh.devices[0, 0, :]})
    n_section, n_dp, n_seq = mesh.devices.shape
    shape = (n_section, n_x, n_dp // n_x, n_seq // n_core, n_core)
    return Mesh(mesh.devices.reshape(shape), ("section", "x", "y", "zl", "core"))


def solution(mesh):
    fine = split_mesh(mesh)
    dp, seq = ("x", "y"), SEQ_AXES
    in_specs = (P("section", dp, seq, None), P(dp, seq, None), P("section", dp, None))
    out_specs = (P("section", dp, seq, None), P("section", dp, None))
    return jax.shard_map(local, mesh=fine, in_specs=in_specs, out_specs=out_specs, check_vma=False)
```

```python
import jax
import jax.numpy as jnp
from jax import lax
from jax.sharding import Mesh, PartitionSpec as P

DILATION_STEP = 16
SEQ_AXES = ("zl", "core")


def with_halo(array, sides, width):
    for axis, dim in sides:
        count, length = (lax.axis_size(axis), array.shape[dim])
        up = [(i, (i + 1) % count) for i in range(count - 1)]
        down = [(j, i) for i, j in up]
        last = lax.slice_in_dim(array, length - width, length, axis=dim)
        initial = lax.slice_in_dim(array, 0, width, axis=dim)
        before = lax.ppermute(last, axis, up)
        after = lax.ppermute(initial, axis, down)
        array = jnp.concatenate([before, array, after], axis=dim)
    return array


def from_behind(value, axis, steps):
    count = lax.axis_size(axis)
    initial, last = (max(0, -steps), min(count, count - steps))
    return lax.ppermute(value, axis, [(source, source + steps) for source in range(initial, last)])


def gelu_gate(value):
    inner = 0.7978845608 * (value + 0.044715 * value * value * value)
    return 0.5 * value * (1.0 + jnp.tanh(inner))


def gelu_derivative(value):
    inner = 0.7978845608 * (value + 0.044715 * value * value * value)
    tangent = jnp.tanh(inner)
    return 0.5 * (1.0 + tangent) + 0.5 * value * (1.0 - tangent * tangent) * 0.7978845608 * (
        1.0 + 0.134145 * value * value
    )


def select_position(array, position_index):
    return lax.dynamic_index_in_dim(array, position_index, 0, keepdims=False)


def local(saved_inputs, pooled_adjoint, weights):
    section_id = lax.axis_index("section")
    is_last = section_id == lax.axis_size("section") - 1
    batch_rows = saved_inputs.shape[2]
    channel_width = weights.shape[2] // 3
    dilation_amount = DILATION_STEP
    full_kernel = lax.all_gather(weights[0], "y", axis=0, tiled=True)
    full_kernel = lax.all_gather(full_kernel, "x", axis=0, tiled=True)
    value_rows = saved_inputs[0].astype(jnp.float32)
    norm_scale = lax.rsqrt(jnp.mean(value_rows * value_rows, axis=-1, keepdims=True) + 1e-05)
    normalized_input = value_rows * norm_scale
    layer_activation = gelu_gate(normalized_input).astype(jnp.bfloat16)
    slope = gelu_derivative(normalized_input)
    upsampled = jnp.repeat(pooled_adjoint, 2, axis=1) * 0.5
    activation_widened = with_halo(layer_activation, ((SEQ_AXES, 1),), dilation_amount)

    def block(cotangent_state):
        cotangent_widened = with_halo(cotangent_state, ((SEQ_AXES, 1),), dilation_amount)
        cotangent_kernel_taps = jnp.concatenate(
            [
                cotangent_widened[
                    :,
                    (2 - kernel_offset) * dilation_amount : (2 - kernel_offset) * dilation_amount
                    + batch_rows,
                ]
                for kernel_offset in range(3)
            ],
            axis=-1,
        )
        reverse_propagate = jnp.einsum(
            "npj,cj->npc", cotangent_kernel_taps, full_kernel, preferred_element_type=jnp.float32
        )
        derivative_gradient = reverse_propagate * slope
        centered_average = jnp.mean(derivative_gradient * normalized_input, axis=-1, keepdims=True)
        return (
            cotangent_state.astype(jnp.float32)
            + norm_scale * (derivative_gradient - normalized_input * centered_average)
        ).astype(jnp.bfloat16)

    upper_output = block(upsampled)
    incoming = from_behind(upper_output, "section", -1)
    cotangent_state = jnp.where(is_last, upsampled, incoming)
    results = block(cotangent_state)
    activation_kernel_taps = jnp.stack(
        [
            activation_widened[
                :, kernel_offset * dilation_amount : kernel_offset * dilation_amount + batch_rows
            ]
            for kernel_offset in range(3)
        ],
        axis=0,
    )
    grad_total = jnp.einsum(
        "knpc,npo->cko", activation_kernel_taps, cotangent_state, preferred_element_type=jnp.float32
    ).reshape(channel_width, 3 * channel_width)
    micro_batch = saved_inputs.shape[1]
    n_dp = lax.axis_size(("x", "y"))
    n_zl = lax.axis_size("zl")
    core_index = lax.axis_index("core")
    swap = [(0, 1), (1, 0)]
    owned_rows = channel_width // n_dp
    half = 3 * channel_width // 2
    own_half = lax.dynamic_slice_in_dim(grad_total, core_index * half, half, axis=1)
    other_half = lax.dynamic_slice_in_dim(grad_total, (1 - core_index) * half, half, axis=1)
    chip_half = own_half + lax.ppermute(other_half, "core", swap)
    pieces = chip_half.astype(jnp.bfloat16).reshape(n_dp, owned_rows, half)
    received = lax.all_to_all(pieces, ("x", "y"), 0, 0, tiled=True)
    owned = jnp.sum(received.astype(jnp.float32), axis=0)
    column_chunk = half // n_zl
    owned = owned.reshape(owned_rows, n_zl, column_chunk).transpose(1, 0, 2)
    summed = jnp.sum(lax.all_to_all(owned, "zl", 0, 0, tiled=True), axis=0)
    chunk_grad = (summed / (micro_batch * n_dp)).astype(jnp.bfloat16)
    half_grad = lax.all_gather(chunk_grad, "zl", axis=1, tiled=True)
    partner_grad = lax.ppermute(half_grad, "core", swap)
    weight_grad = jnp.where(
        core_index == 0,
        jnp.concatenate([half_grad, partner_grad], axis=1),
        jnp.concatenate([partner_grad, half_grad], axis=1),
    )
    return (results[None], weight_grad[None])


def split_mesh(mesh):
    dp_devices = mesh.devices[0, :, 0]
    n_x = len({device.coords[0] for device in dp_devices})
    n_core = len({device.core_on_chip for device in mesh.devices[0, 0, :]})
    n_section, n_dp, n_seq = mesh.devices.shape
    shape = (n_section, n_x, n_dp // n_x, n_seq // n_core, n_core)
    return Mesh(mesh.devices.reshape(shape), ("section", "x", "y", "zl", "core"))


def solution(mesh):
    fine = split_mesh(mesh)
    dp, seq = ("x", "y"), SEQ_AXES
    in_specs = (P("section", dp, seq, None), P(dp, seq, None), P("section", dp, None))
    out_specs = (P("section", dp, seq, None), P("section", dp, None))
    return jax.shard_map(local, mesh=fine, in_specs=in_specs, out_specs=out_specs, check_vma=False)
```

```python
import jax
import jax.numpy as jnp
from jax import lax
from jax.sharding import Mesh, PartitionSpec as P

DILATION_STEP = 16
SEQ_AXES = ("zl", "core")


def with_halo(array, sides, width):
    for axis, dim in sides:
        count, length = (lax.axis_size(axis), array.shape[dim])
        up = [(i, (i + 1) % count) for i in range(count - 1)]
        down = [(j, i) for i, j in up]
        last = lax.slice_in_dim(array, length - width, length, axis=dim)
        initial = lax.slice_in_dim(array, 0, width, axis=dim)
        before = lax.ppermute(last, axis, up)
        after = lax.ppermute(initial, axis, down)
        array = jnp.concatenate([before, array, after], axis=dim)
    return array


def from_behind(value, axis, steps):
    count = lax.axis_size(axis)
    initial, last = (max(0, -steps), min(count, count - steps))
    return lax.ppermute(value, axis, [(source, source + steps) for source in range(initial, last)])


def gelu_gate(value):
    inner = 0.7978845608 * (value + 0.044715 * value * value * value)
    return 0.5 * value * (1.0 + jnp.tanh(inner))


def gelu_derivative(value):
    inner = 0.7978845608 * (value + 0.044715 * value * value * value)
    tangent = jnp.tanh(inner)
    return 0.5 * (1.0 + tangent) + 0.5 * value * (1.0 - tangent * tangent) * 0.7978845608 * (
        1.0 + 0.134145 * value * value
    )


def select_position(array, position_index):
    return lax.dynamic_index_in_dim(array, position_index, 0, keepdims=False)


def local(saved_inputs, pooled_adjoint, weights):
    section_id = lax.axis_index("section")
    is_last = section_id == lax.axis_size("section") - 1
    batch_rows = saved_inputs.shape[2]
    channel_width = weights.shape[2] // 3
    dilation_amount = DILATION_STEP
    full_kernel = lax.all_gather(weights[0], "y", axis=0, tiled=True)
    full_kernel = lax.all_gather(full_kernel, "x", axis=0, tiled=True)
    value_rows = saved_inputs[0].astype(jnp.float32)
    norm_scale = lax.rsqrt(jnp.mean(value_rows * value_rows, axis=-1, keepdims=True) + 1e-05)
    normalized_input = value_rows * norm_scale
    layer_activation = gelu_gate(normalized_input).astype(jnp.bfloat16)
    slope = gelu_derivative(normalized_input)
    upsampled = jnp.repeat(pooled_adjoint, 2, axis=1) * 0.5
    activation_widened = with_halo(layer_activation, ((SEQ_AXES, 1),), dilation_amount)

    def block(cotangent_state):
        cotangent_widened = with_halo(cotangent_state, ((SEQ_AXES, 1),), dilation_amount)
        cotangent_kernel_taps = jnp.concatenate(
            [
                cotangent_widened[
                    :,
                    (2 - kernel_offset) * dilation_amount : (2 - kernel_offset) * dilation_amount
                    + batch_rows,
                ]
                for kernel_offset in range(3)
            ],
            axis=-1,
        )
        reverse_propagate = jnp.einsum(
            "npj,cj->npc", cotangent_kernel_taps, full_kernel, preferred_element_type=jnp.float32
        )
        derivative_gradient = reverse_propagate * slope
        centered_average = jnp.mean(derivative_gradient * normalized_input, axis=-1, keepdims=True)
        return (
            cotangent_state.astype(jnp.float32)
            + norm_scale * (derivative_gradient - normalized_input * centered_average)
        ).astype(jnp.bfloat16)

    upper_output = block(upsampled)
    incoming = from_behind(upper_output, "section", -1)
    cotangent_state = jnp.where(is_last, upsampled, incoming)
    results = block(cotangent_state)
    activation_kernel_taps = jnp.stack(
        [
            activation_widened[
                :, kernel_offset * dilation_amount : kernel_offset * dilation_amount + batch_rows
            ]
            for kernel_offset in range(3)
        ],
        axis=0,
    )
    grad_total = jnp.einsum(
        "knpc,npo->cko", activation_kernel_taps, cotangent_state, preferred_element_type=jnp.float32
    ).reshape(channel_width, 3 * channel_width)
    micro_batch = saved_inputs.shape[1]
    n_dp = lax.axis_size(("x", "y"))
    n_zl = lax.axis_size("zl")
    core_index = lax.axis_index("core")
    swap = [(0, 1), (1, 0)]
    owned_rows = channel_width // n_dp
    half = 3 * channel_width // 2
    own_half = lax.dynamic_slice_in_dim(grad_total, core_index * half, half, axis=1)
    other_half = lax.dynamic_slice_in_dim(grad_total, (1 - core_index) * half, half, axis=1)
    chip_half = own_half + lax.ppermute(other_half, "core", swap)
    pieces = chip_half.astype(jnp.bfloat16).reshape(n_dp, owned_rows, half)
    received = lax.all_to_all(pieces, ("x", "y"), 0, 0, tiled=True)
    owned = jnp.sum(received.astype(jnp.float32), axis=0)
    copies = jnp.broadcast_to(owned[None], (n_zl, owned_rows, half))
    summed = jnp.sum(lax.all_to_all(copies, "zl", 0, 0, tiled=True), axis=0)
    half_grad = (summed / (micro_batch * n_dp)).astype(jnp.bfloat16)
    partner_grad = lax.ppermute(half_grad, "core", swap)
    weight_grad = jnp.where(
        core_index == 0,
        jnp.concatenate([half_grad, partner_grad], axis=1),
        jnp.concatenate([partner_grad, half_grad], axis=1),
    )
    return (results[None], weight_grad[None])


def split_mesh(mesh):
    dp_devices = mesh.devices[0, :, 0]
    n_x = len({device.coords[0] for device in dp_devices})
    n_core = len({device.core_on_chip for device in mesh.devices[0, 0, :]})
    n_section, n_dp, n_seq = mesh.devices.shape
    shape = (n_section, n_x, n_dp // n_x, n_seq // n_core, n_core)
    return Mesh(mesh.devices.reshape(shape), ("section", "x", "y", "zl", "core"))


def solution(mesh):
    fine = split_mesh(mesh)
    dp, seq = ("x", "y"), SEQ_AXES
    in_specs = (P("section", dp, seq, None), P(dp, seq, None), P("section", dp, None))
    out_specs = (P("section", dp, seq, None), P("section", dp, None))
    return jax.shard_map(local, mesh=fine, in_specs=in_specs, out_specs=out_specs, check_vma=False)
```

```python
import jax
import jax.numpy as jnp
from jax import lax
from jax.sharding import Mesh, PartitionSpec as P

DILATION_STEP = 16
SEQ_AXES = ("zl", "core")


def with_halo(array, sides, width):
    for axis, dim in sides:
        count, length = (lax.axis_size(axis), array.shape[dim])
        up = [(i, (i + 1) % count) for i in range(count - 1)]
        down = [(j, i) for i, j in up]
        last = lax.slice_in_dim(array, length - width, length, axis=dim)
        initial = lax.slice_in_dim(array, 0, width, axis=dim)
        before = lax.ppermute(last, axis, up)
        after = lax.ppermute(initial, axis, down)
        array = jnp.concatenate([before, array, after], axis=dim)
    return array


def from_behind(value, axis, steps):
    count = lax.axis_size(axis)
    initial, last = (max(0, -steps), min(count, count - steps))
    return lax.ppermute(value, axis, [(source, source + steps) for source in range(initial, last)])


def gelu_gate(value):
    inner = 0.7978845608 * (value + 0.044715 * value * value * value)
    return 0.5 * value * (1.0 + jnp.tanh(inner))


def gelu_derivative(value):
    inner = 0.7978845608 * (value + 0.044715 * value * value * value)
    tangent = jnp.tanh(inner)
    return 0.5 * (1.0 + tangent) + 0.5 * value * (1.0 - tangent * tangent) * 0.7978845608 * (
        1.0 + 0.134145 * value * value
    )


def select_position(array, position_index):
    return lax.dynamic_index_in_dim(array, position_index, 0, keepdims=False)


def local(saved_inputs, pooled_adjoint, weights):
    section_id = lax.axis_index("section")
    is_last = section_id == lax.axis_size("section") - 1
    batch_rows = saved_inputs.shape[2]
    channel_width = weights.shape[2] // 3
    dilation_amount = DILATION_STEP
    kernel_core = lax.axis_index("core")
    kernel_half = weights.shape[2] // 2
    own_columns = lax.dynamic_slice_in_dim(weights[0], kernel_core * kernel_half, kernel_half, axis=1)
    own_columns = lax.all_gather(own_columns, "y", axis=0, tiled=True)
    own_columns = lax.all_gather(own_columns, "x", axis=0, tiled=True)
    partner_columns = lax.ppermute(own_columns, "core", [(0, 1), (1, 0)])
    full_kernel = jnp.where(
        kernel_core == 0,
        jnp.concatenate([own_columns, partner_columns], axis=1),
        jnp.concatenate([partner_columns, own_columns], axis=1),
    )
    value_rows = saved_inputs[0].astype(jnp.float32)
    norm_scale = lax.rsqrt(jnp.mean(value_rows * value_rows, axis=-1, keepdims=True) + 1e-05)
    normalized_input = value_rows * norm_scale
    layer_activation = gelu_gate(normalized_input).astype(jnp.bfloat16)
    slope = gelu_derivative(normalized_input)
    upsampled = jnp.repeat(pooled_adjoint, 2, axis=1) * 0.5
    activation_widened = with_halo(layer_activation, ((SEQ_AXES, 1),), dilation_amount)

    def block(cotangent_state):
        cotangent_widened = with_halo(cotangent_state, ((SEQ_AXES, 1),), dilation_amount)
        cotangent_kernel_taps = jnp.concatenate(
            [
                cotangent_widened[
                    :,
                    (2 - kernel_offset) * dilation_amount : (2 - kernel_offset) * dilation_amount
                    + batch_rows,
                ]
                for kernel_offset in range(3)
            ],
            axis=-1,
        )
        reverse_propagate = jnp.einsum(
            "npj,cj->npc", cotangent_kernel_taps, full_kernel, preferred_element_type=jnp.float32
        )
        derivative_gradient = reverse_propagate * slope
        centered_average = jnp.mean(derivative_gradient * normalized_input, axis=-1, keepdims=True)
        return (
            cotangent_state.astype(jnp.float32)
            + norm_scale * (derivative_gradient - normalized_input * centered_average)
        ).astype(jnp.bfloat16)

    upper_output = block(upsampled)
    incoming = from_behind(upper_output, "section", -1)
    cotangent_state = jnp.where(is_last, upsampled, incoming)
    results = block(cotangent_state)
    activation_kernel_taps = jnp.stack(
        [
            activation_widened[
                :, kernel_offset * dilation_amount : kernel_offset * dilation_amount + batch_rows
            ]
            for kernel_offset in range(3)
        ],
        axis=0,
    )
    grad_total = jnp.einsum(
        "knpc,npo->cko", activation_kernel_taps, cotangent_state, preferred_element_type=jnp.float32
    ).reshape(channel_width, 3 * channel_width)
    micro_batch = saved_inputs.shape[1]
    n_dp = lax.axis_size(("x", "y"))
    n_zl = lax.axis_size("zl")
    core_index = lax.axis_index("core")
    swap = [(0, 1), (1, 0)]
    owned_rows = channel_width // n_dp
    half = 3 * channel_width // 2
    own_half = lax.dynamic_slice_in_dim(grad_total, core_index * half, half, axis=1)
    other_half = lax.dynamic_slice_in_dim(grad_total, (1 - core_index) * half, half, axis=1)
    chip_half = own_half + lax.ppermute(other_half, "core", swap)
    pieces = chip_half.astype(jnp.bfloat16).reshape(n_dp, owned_rows, half)
    received = lax.all_to_all(pieces, ("x", "y"), 0, 0, tiled=True)
    owned = jnp.sum(received.astype(jnp.float32), axis=0)
    copies = jnp.broadcast_to(owned[None], (n_zl, owned_rows, half))
    summed = jnp.sum(lax.all_to_all(copies, "zl", 0, 0, tiled=True), axis=0)
    half_grad = (summed / (micro_batch * n_dp)).astype(jnp.bfloat16)
    partner_grad = lax.ppermute(half_grad, "core", swap)
    weight_grad = jnp.where(
        core_index == 0,
        jnp.concatenate([half_grad, partner_grad], axis=1),
        jnp.concatenate([partner_grad, half_grad], axis=1),
    )
    return (results[None], weight_grad[None])


def split_mesh(mesh):
    dp_devices = mesh.devices[0, :, 0]
    n_x = len({device.coords[0] for device in dp_devices})
    n_core = len({device.core_on_chip for device in mesh.devices[0, 0, :]})
    n_section, n_dp, n_seq = mesh.devices.shape
    shape = (n_section, n_x, n_dp // n_x, n_seq // n_core, n_core)
    return Mesh(mesh.devices.reshape(shape), ("section", "x", "y", "zl", "core"))


def solution(mesh):
    fine = split_mesh(mesh)
    dp, seq = ("x", "y"), SEQ_AXES
    in_specs = (P("section", dp, seq, None), P(dp, seq, None), P("section", dp, None))
    out_specs = (P("section", dp, seq, None), P("section", dp, None))
    return jax.shard_map(local, mesh=fine, in_specs=in_specs, out_specs=out_specs, check_vma=False)
```

```python
import jax
import jax.numpy as jnp
from jax import lax
from jax.sharding import Mesh, PartitionSpec as P

DILATION_STEP = 16
SEQ_AXES = ("zl", "core")


def with_halo(array, sides, width):
    for axis, dim in sides:
        count, length = (lax.axis_size(axis), array.shape[dim])
        up = [(i, (i + 1) % count) for i in range(count - 1)]
        down = [(j, i) for i, j in up]
        last = lax.slice_in_dim(array, length - width, length, axis=dim)
        initial = lax.slice_in_dim(array, 0, width, axis=dim)
        before = lax.ppermute(last, axis, up)
        after = lax.ppermute(initial, axis, down)
        array = jnp.concatenate([before, array, after], axis=dim)
    return array


def from_behind(value, axis, steps):
    count = lax.axis_size(axis)
    initial, last = (max(0, -steps), min(count, count - steps))
    return lax.ppermute(value, axis, [(source, source + steps) for source in range(initial, last)])


def gelu_gate(value):
    inner = 0.7978845608 * (value + 0.044715 * value * value * value)
    return 0.5 * value * (1.0 + jnp.tanh(inner))


def gelu_derivative(value):
    inner = 0.7978845608 * (value + 0.044715 * value * value * value)
    tangent = jnp.tanh(inner)
    return 0.5 * (1.0 + tangent) + 0.5 * value * (1.0 - tangent * tangent) * 0.7978845608 * (
        1.0 + 0.134145 * value * value
    )


def select_position(array, position_index):
    return lax.dynamic_index_in_dim(array, position_index, 0, keepdims=False)


def local(saved_inputs, pooled_adjoint, weights):
    section_id = lax.axis_index("section")
    is_last = section_id == lax.axis_size("section") - 1
    batch_rows = saved_inputs.shape[2]
    channel_width = weights.shape[2] // 3
    dilation_amount = DILATION_STEP
    kernel_core = lax.axis_index("core")
    kernel_half = weights.shape[2] // 2
    own_columns = lax.dynamic_slice_in_dim(weights[0], kernel_core * kernel_half, kernel_half, axis=1)
    own_columns = lax.all_gather(own_columns, "y", axis=0, tiled=True)
    own_columns = lax.all_gather(own_columns, "x", axis=0, tiled=True)
    partner_columns = lax.ppermute(own_columns, "core", [(0, 1), (1, 0)])
    full_kernel = jnp.where(
        kernel_core == 0,
        jnp.concatenate([own_columns, partner_columns], axis=1),
        jnp.concatenate([partner_columns, own_columns], axis=1),
    )
    seq_index = lax.axis_index(SEQ_AXES)
    sequence_length = lax.axis_size(SEQ_AXES) * batch_rows
    inputs_widened = with_halo(saved_inputs[0], ((SEQ_AXES, 1),), dilation_amount)
    upsampled = jnp.repeat(pooled_adjoint, 2, axis=1) * 0.5
    upsampled_widened = with_halo(upsampled, ((SEQ_AXES, 1),), 2 * dilation_amount)
    value_rows = inputs_widened.astype(jnp.float32)
    norm_scale = lax.rsqrt(jnp.mean(value_rows * value_rows, axis=-1, keepdims=True) + 1e-05)
    normalized_input = value_rows * norm_scale
    activation_widened = gelu_gate(normalized_input).astype(jnp.bfloat16)
    slope = gelu_derivative(normalized_input)
    wide_rows = batch_rows + 2 * dilation_amount

    def block(cotangent_widened, cotangent_state, scale, normalized, derivative, rows):
        cotangent_kernel_taps = jnp.concatenate(
            [
                cotangent_widened[
                    :,
                    (2 - kernel_offset) * dilation_amount : (2 - kernel_offset) * dilation_amount
                    + rows,
                ]
                for kernel_offset in range(3)
            ],
            axis=-1,
        )
        reverse_propagate = jnp.einsum(
            "npj,cj->npc", cotangent_kernel_taps, full_kernel, preferred_element_type=jnp.float32
        )
        derivative_gradient = reverse_propagate * derivative
        centered_average = jnp.mean(derivative_gradient * normalized, axis=-1, keepdims=True)
        return (
            cotangent_state.astype(jnp.float32)
            + scale * (derivative_gradient - normalized * centered_average)
        ).astype(jnp.bfloat16)

    upsampled_halo = upsampled_widened[:, dilation_amount : dilation_amount + wide_rows]
    upper_output = block(
        upsampled_widened, upsampled_halo, norm_scale, normalized_input, slope, wide_rows
    )
    position = seq_index * batch_rows - dilation_amount + jnp.arange(wide_rows)
    inside = (position >= 0) & (position < sequence_length)
    upper_output = jnp.where(inside[None, :, None], upper_output, jnp.zeros_like(upper_output))
    incoming = from_behind(upper_output, "section", -1)
    cotangent_widened = jnp.where(is_last, upsampled_halo, incoming)
    centre = slice(dilation_amount, dilation_amount + batch_rows)
    cotangent_state = cotangent_widened[:, centre]
    results = block(
        cotangent_widened,
        cotangent_state,
        norm_scale[:, centre],
        normalized_input[:, centre],
        slope[:, centre],
        batch_rows,
    )
    activation_kernel_taps = jnp.stack(
        [
            activation_widened[
                :, kernel_offset * dilation_amount : kernel_offset * dilation_amount + batch_rows
            ]
            for kernel_offset in range(3)
        ],
        axis=0,
    )
    grad_total = jnp.einsum(
        "knpc,npo->cko", activation_kernel_taps, cotangent_state, preferred_element_type=jnp.float32
    ).reshape(channel_width, 3 * channel_width)
    micro_batch = saved_inputs.shape[1]
    n_dp = lax.axis_size(("x", "y"))
    n_zl = lax.axis_size("zl")
    core_index = lax.axis_index("core")
    swap = [(0, 1), (1, 0)]
    owned_rows = channel_width // n_dp
    half = 3 * channel_width // 2
    own_half = lax.dynamic_slice_in_dim(grad_total, core_index * half, half, axis=1)
    other_half = lax.dynamic_slice_in_dim(grad_total, (1 - core_index) * half, half, axis=1)
    chip_half = own_half + lax.ppermute(other_half, "core", swap)
    pieces = chip_half.astype(jnp.bfloat16).reshape(n_dp, owned_rows, half)
    received = lax.all_to_all(pieces, ("x", "y"), 0, 0, tiled=True)
    owned = jnp.sum(received.astype(jnp.float32), axis=0)
    copies = jnp.broadcast_to(owned[None], (n_zl, owned_rows, half))
    summed = jnp.sum(lax.all_to_all(copies, "zl", 0, 0, tiled=True), axis=0)
    half_grad = (summed / (micro_batch * n_dp)).astype(jnp.bfloat16)
    partner_grad = lax.ppermute(half_grad, "core", swap)
    weight_grad = jnp.where(
        core_index == 0,
        jnp.concatenate([half_grad, partner_grad], axis=1),
        jnp.concatenate([partner_grad, half_grad], axis=1),
    )
    return (results[None], weight_grad[None])


def split_mesh(mesh):
    dp_devices = mesh.devices[0, :, 0]
    n_x = len({device.coords[0] for device in dp_devices})
    n_core = len({device.core_on_chip for device in mesh.devices[0, 0, :]})
    n_section, n_dp, n_seq = mesh.devices.shape
    shape = (n_section, n_x, n_dp // n_x, n_seq // n_core, n_core)
    return Mesh(mesh.devices.reshape(shape), ("section", "x", "y", "zl", "core"))


def solution(mesh):
    fine = split_mesh(mesh)
    dp, seq = ("x", "y"), SEQ_AXES
    in_specs = (P("section", dp, seq, None), P(dp, seq, None), P("section", dp, None))
    out_specs = (P("section", dp, seq, None), P("section", dp, None))
    return jax.shard_map(local, mesh=fine, in_specs=in_specs, out_specs=out_specs, check_vma=False)
```

```python
import jax
import jax.numpy as jnp
from jax import lax
from jax.sharding import Mesh, PartitionSpec as P

DILATION_STEP = 16
SEQ_AXES = ("zl", "core")


def with_halo(array, sides, width):
    for axis, dim in sides:
        count, length = (lax.axis_size(axis), array.shape[dim])
        up = [(i, (i + 1) % count) for i in range(count - 1)]
        down = [(j, i) for i, j in up]
        last = lax.slice_in_dim(array, length - width, length, axis=dim)
        initial = lax.slice_in_dim(array, 0, width, axis=dim)
        before = lax.ppermute(last, axis, up)
        after = lax.ppermute(initial, axis, down)
        array = jnp.concatenate([before, array, after], axis=dim)
    return array


def from_behind(value, axis, steps):
    count = lax.axis_size(axis)
    initial, last = (max(0, -steps), min(count, count - steps))
    return lax.ppermute(value, axis, [(source, source + steps) for source in range(initial, last)])


def gelu_gate(value):
    inner = 0.7978845608 * (value + 0.044715 * value * value * value)
    return 0.5 * value * (1.0 + jnp.tanh(inner))


def gelu_derivative(value):
    inner = 0.7978845608 * (value + 0.044715 * value * value * value)
    tangent = jnp.tanh(inner)
    return 0.5 * (1.0 + tangent) + 0.5 * value * (1.0 - tangent * tangent) * 0.7978845608 * (
        1.0 + 0.134145 * value * value
    )


def select_position(array, position_index):
    return lax.dynamic_index_in_dim(array, position_index, 0, keepdims=False)


def local(saved_inputs, pooled_adjoint, weights):
    section_id = lax.axis_index("section")
    is_last = section_id == lax.axis_size("section") - 1
    batch_rows = saved_inputs.shape[2]
    channel_width = weights.shape[2] // 3
    dilation_amount = DILATION_STEP
    kernel_core = lax.axis_index("core")
    kernel_half = weights.shape[2] // 2
    own_columns = lax.dynamic_slice_in_dim(weights[0], kernel_core * kernel_half, kernel_half, axis=1)
    own_columns = lax.all_gather(own_columns, "y", axis=0, tiled=True)
    own_columns = lax.all_gather(own_columns, "x", axis=0, tiled=True)
    partner_columns = lax.ppermute(own_columns, "core", [(0, 1), (1, 0)])
    full_kernel = jnp.where(
        kernel_core == 0,
        jnp.concatenate([own_columns, partner_columns], axis=1),
        jnp.concatenate([partner_columns, own_columns], axis=1),
    )
    seq_index = lax.axis_index(SEQ_AXES)
    sequence_length = lax.axis_size(SEQ_AXES) * batch_rows
    inputs_widened = with_halo(saved_inputs[0], ((SEQ_AXES, 1),), dilation_amount)
    upsampled = jnp.repeat(pooled_adjoint, 2, axis=1) * 0.5
    upsampled_widened = with_halo(upsampled, ((SEQ_AXES, 1),), 2 * dilation_amount)
    value_rows = inputs_widened.astype(jnp.float32)
    norm_scale = lax.rsqrt(jnp.mean(value_rows * value_rows, axis=-1, keepdims=True) + 1e-05)
    normalized_input = value_rows * norm_scale
    activation_widened = gelu_gate(normalized_input).astype(jnp.bfloat16)
    slope = gelu_derivative(normalized_input)
    wide_rows = batch_rows + 2 * dilation_amount

    def block(cotangent_widened, cotangent_state, scale, normalized, derivative, rows):
        cotangent_kernel_taps = jnp.concatenate(
            [
                cotangent_widened[
                    :,
                    (2 - kernel_offset) * dilation_amount : (2 - kernel_offset) * dilation_amount
                    + rows,
                ]
                for kernel_offset in range(3)
            ],
            axis=-1,
        )
        reverse_propagate = jnp.einsum(
            "npj,cj->npc", cotangent_kernel_taps, full_kernel, preferred_element_type=jnp.float32
        )
        derivative_gradient = reverse_propagate * derivative
        centered_average = jnp.mean(derivative_gradient * normalized, axis=-1, keepdims=True)
        return (
            cotangent_state.astype(jnp.float32)
            + scale * (derivative_gradient - normalized * centered_average)
        ).astype(jnp.bfloat16)

    upsampled_halo = upsampled_widened[:, dilation_amount : dilation_amount + wide_rows]
    upper_output = block(
        upsampled_widened, upsampled_halo, norm_scale, normalized_input, slope, wide_rows
    )
    position = seq_index * batch_rows - dilation_amount + jnp.arange(wide_rows)
    inside = (position >= 0) & (position < sequence_length)
    upper_output = jnp.where(inside[None, :, None], upper_output, jnp.zeros_like(upper_output))
    incoming = from_behind(upper_output, "section", -1)
    cotangent_widened = jnp.where(is_last, upsampled_halo, incoming)
    centre = slice(dilation_amount, dilation_amount + batch_rows)
    cotangent_state = cotangent_widened[:, centre]
    results = block(
        cotangent_widened,
        cotangent_state,
        norm_scale[:, centre],
        normalized_input[:, centre],
        slope[:, centre],
        batch_rows,
    )
    activation_kernel_taps = jnp.stack(
        [
            activation_widened[
                :, kernel_offset * dilation_amount : kernel_offset * dilation_amount + batch_rows
            ]
            for kernel_offset in range(3)
        ],
        axis=0,
    )
    grad_total = jnp.einsum(
        "knpc,npo->cko", activation_kernel_taps, cotangent_state, preferred_element_type=jnp.float32
    ).reshape(channel_width, 3 * channel_width)
    micro_batch = saved_inputs.shape[1]
    n_dp = lax.axis_size(("x", "y"))
    n_zl = lax.axis_size("zl")
    core_index = lax.axis_index("core")
    swap = [(0, 1), (1, 0)]
    owned_rows = channel_width // n_dp
    n_core = lax.axis_size("core")
    rows_per_core = owned_rows // n_core
    grouped = grad_total.reshape(n_dp, n_core, rows_per_core, 3 * channel_width)
    own_rows = lax.dynamic_index_in_dim(grouped, core_index, axis=1, keepdims=False)
    other_rows = lax.dynamic_index_in_dim(grouped, 1 - core_index, axis=1, keepdims=False)
    chip_rows = own_rows + lax.ppermute(other_rows, "core", swap)
    received = lax.all_to_all(chip_rows.astype(jnp.bfloat16), ("x", "y"), 0, 0, tiled=True)
    owned = jnp.sum(received.astype(jnp.float32), axis=0)
    copies = jnp.broadcast_to(owned[None], (n_zl, rows_per_core, 3 * channel_width))
    summed = jnp.sum(lax.all_to_all(copies, "zl", 0, 0, tiled=True), axis=0)
    part_grad = (summed / (micro_batch * n_dp)).astype(jnp.bfloat16)
    partner_grad = lax.ppermute(part_grad, "core", swap)
    weight_grad = jnp.where(
        core_index == 0,
        jnp.concatenate([part_grad, partner_grad], axis=0),
        jnp.concatenate([partner_grad, part_grad], axis=0),
    )
    return (results[None], weight_grad[None])


def split_mesh(mesh):
    dp_devices = mesh.devices[0, :, 0]
    n_x = len({device.coords[0] for device in dp_devices})
    n_core = len({device.core_on_chip for device in mesh.devices[0, 0, :]})
    n_section, n_dp, n_seq = mesh.devices.shape
    shape = (n_section, n_x, n_dp // n_x, n_seq // n_core, n_core)
    return Mesh(mesh.devices.reshape(shape), ("section", "x", "y", "zl", "core"))


def solution(mesh):
    fine = split_mesh(mesh)
    dp, seq = ("x", "y"), SEQ_AXES
    in_specs = (P("section", dp, seq, None), P(dp, seq, None), P("section", dp, None))
    out_specs = (P("section", dp, seq, None), P("section", dp, None))
    return jax.shard_map(local, mesh=fine, in_specs=in_specs, out_specs=out_specs, check_vma=False)
```

```python
import jax
import jax.numpy as jnp
from jax import lax
from jax.sharding import Mesh, PartitionSpec as P

DILATION_STEP = 16
SEQ_AXES = ("zl", "core")


def with_halo(array, sides, width):
    for axis, dim in sides:
        count, length = (lax.axis_size(axis), array.shape[dim])
        up = [(i, (i + 1) % count) for i in range(count - 1)]
        down = [(j, i) for i, j in up]
        last = lax.slice_in_dim(array, length - width, length, axis=dim)
        initial = lax.slice_in_dim(array, 0, width, axis=dim)
        before = lax.ppermute(last, axis, up)
        after = lax.ppermute(initial, axis, down)
        array = jnp.concatenate([before, array, after], axis=dim)
    return array


def from_behind(value, axis, steps):
    count = lax.axis_size(axis)
    initial, last = (max(0, -steps), min(count, count - steps))
    return lax.ppermute(value, axis, [(source, source + steps) for source in range(initial, last)])


def gelu_gate(value):
    inner = 0.7978845608 * (value + 0.044715 * value * value * value)
    return 0.5 * value * (1.0 + jnp.tanh(inner))


def gelu_derivative(value):
    inner = 0.7978845608 * (value + 0.044715 * value * value * value)
    tangent = jnp.tanh(inner)
    return 0.5 * (1.0 + tangent) + 0.5 * value * (1.0 - tangent * tangent) * 0.7978845608 * (
        1.0 + 0.134145 * value * value
    )


def select_position(array, position_index):
    return lax.dynamic_index_in_dim(array, position_index, 0, keepdims=False)


def local(saved_inputs, pooled_adjoint, weights):
    section_id = lax.axis_index("section")
    is_last = section_id == lax.axis_size("section") - 1
    batch_rows = saved_inputs.shape[2]
    channel_width = weights.shape[2] // 3
    dilation_amount = DILATION_STEP
    kernel_core = lax.axis_index("core")
    kernel_half = weights.shape[2] // 2
    own_columns = lax.dynamic_slice_in_dim(weights[0], kernel_core * kernel_half, kernel_half, axis=1)
    own_columns = lax.all_gather(own_columns, "y", axis=0, tiled=True)
    own_columns = lax.all_gather(own_columns, "x", axis=0, tiled=True)
    partner_columns = lax.ppermute(own_columns, "core", [(0, 1), (1, 0)])
    full_kernel = jnp.where(
        kernel_core == 0,
        jnp.concatenate([own_columns, partner_columns], axis=1),
        jnp.concatenate([partner_columns, own_columns], axis=1),
    )
    seq_index = lax.axis_index(SEQ_AXES)
    sequence_length = lax.axis_size(SEQ_AXES) * batch_rows
    inputs_widened = with_halo(saved_inputs[0], ((SEQ_AXES, 1),), dilation_amount)
    upsampled = jnp.repeat(pooled_adjoint, 2, axis=1) * 0.5
    upsampled_widened = with_halo(upsampled, ((SEQ_AXES, 1),), 2 * dilation_amount)
    value_rows = inputs_widened.astype(jnp.float32)
    norm_scale = lax.rsqrt(jnp.mean(value_rows * value_rows, axis=-1, keepdims=True) + 1e-05)
    normalized_input = value_rows * norm_scale
    activation_widened = gelu_gate(normalized_input).astype(jnp.bfloat16)
    slope = gelu_derivative(normalized_input)
    wide_rows = batch_rows + 2 * dilation_amount

    def block(cotangent_widened, cotangent_state, scale, normalized, derivative, rows):
        cotangent_kernel_taps = jnp.concatenate(
            [
                cotangent_widened[
                    :,
                    (2 - kernel_offset) * dilation_amount : (2 - kernel_offset) * dilation_amount
                    + rows,
                ]
                for kernel_offset in range(3)
            ],
            axis=-1,
        )
        reverse_propagate = jnp.einsum(
            "npj,cj->npc", cotangent_kernel_taps, full_kernel, preferred_element_type=jnp.float32
        )
        derivative_gradient = reverse_propagate * derivative
        centered_average = jnp.mean(derivative_gradient * normalized, axis=-1, keepdims=True)
        return (
            cotangent_state.astype(jnp.float32)
            + scale * (derivative_gradient - normalized * centered_average)
        ).astype(jnp.bfloat16)

    upsampled_halo = upsampled_widened[:, dilation_amount : dilation_amount + wide_rows]
    upper_output = block(
        upsampled_widened, upsampled_halo, norm_scale, normalized_input, slope, wide_rows
    )
    position = seq_index * batch_rows - dilation_amount + jnp.arange(wide_rows)
    inside = (position >= 0) & (position < sequence_length)
    upper_output = jnp.where(inside[None, :, None], upper_output, jnp.zeros_like(upper_output))
    incoming = from_behind(upper_output, "section", -1)
    cotangent_widened = jnp.where(is_last, upsampled_halo, incoming)
    centre = slice(dilation_amount, dilation_amount + batch_rows)
    cotangent_state = cotangent_widened[:, centre]
    results = block(
        cotangent_widened,
        cotangent_state,
        norm_scale[:, centre],
        normalized_input[:, centre],
        slope[:, centre],
        batch_rows,
    )
    activation_kernel_taps = jnp.stack(
        [
            activation_widened[
                :, kernel_offset * dilation_amount : kernel_offset * dilation_amount + batch_rows
            ]
            for kernel_offset in range(3)
        ],
        axis=0,
    )
    grad_total = jnp.einsum(
        "knpc,npo->cko", activation_kernel_taps, cotangent_state, preferred_element_type=jnp.float32
    ).reshape(channel_width, 3 * channel_width)
    micro_batch = saved_inputs.shape[1]
    n_dp = lax.axis_size(("x", "y"))
    n_zl = lax.axis_size("zl")
    core_index = lax.axis_index("core")
    swap = [(0, 1), (1, 0)]
    owned_rows = channel_width // n_dp
    half = 3 * channel_width // 2
    own_half = lax.dynamic_slice_in_dim(grad_total, core_index * half, half, axis=1)
    other_half = lax.dynamic_slice_in_dim(grad_total, (1 - core_index) * half, half, axis=1)
    chip_half = own_half + lax.ppermute(other_half, "core", swap)
    pieces = chip_half.astype(jnp.bfloat16).reshape(n_dp, owned_rows, half)
    received = lax.all_to_all(pieces, ("x", "y"), 0, 0, tiled=True)
    owned = jnp.sum(received.astype(jnp.float32), axis=0)
    copies = jnp.broadcast_to(owned.astype(jnp.bfloat16)[None], (n_zl, owned_rows, half))
    summed = jnp.sum(lax.all_to_all(copies, "zl", 0, 0, tiled=True).astype(jnp.float32), axis=0)
    half_grad = (summed / (micro_batch * n_dp)).astype(jnp.bfloat16)
    partner_grad = lax.ppermute(half_grad, "core", swap)
    weight_grad = jnp.where(
        core_index == 0,
        jnp.concatenate([half_grad, partner_grad], axis=1),
        jnp.concatenate([partner_grad, half_grad], axis=1),
    )
    return (results[None], weight_grad[None])


def split_mesh(mesh):
    dp_devices = mesh.devices[0, :, 0]
    n_x = len({device.coords[0] for device in dp_devices})
    n_core = len({device.core_on_chip for device in mesh.devices[0, 0, :]})
    n_section, n_dp, n_seq = mesh.devices.shape
    shape = (n_section, n_x, n_dp // n_x, n_seq // n_core, n_core)
    return Mesh(mesh.devices.reshape(shape), ("section", "x", "y", "zl", "core"))


def solution(mesh):
    fine = split_mesh(mesh)
    dp, seq = ("x", "y"), SEQ_AXES
    in_specs = (P("section", dp, seq, None), P(dp, seq, None), P("section", dp, None))
    out_specs = (P("section", dp, seq, None), P("section", dp, None))
    return jax.shard_map(local, mesh=fine, in_specs=in_specs, out_specs=out_specs, check_vma=False)
```

```python
import jax
import jax.numpy as jnp
from jax import lax
from jax.sharding import Mesh, PartitionSpec as P

DILATION_STEP = 16
SEQ_AXES = ("zl", "core")


def with_halo(array, sides, width):
    for axis, dim in sides:
        count, length = (lax.axis_size(axis), array.shape[dim])
        up = [(i, (i + 1) % count) for i in range(count - 1)]
        down = [(j, i) for i, j in up]
        last = lax.slice_in_dim(array, length - width, length, axis=dim)
        initial = lax.slice_in_dim(array, 0, width, axis=dim)
        before = lax.ppermute(last, axis, up)
        after = lax.ppermute(initial, axis, down)
        array = jnp.concatenate([before, array, after], axis=dim)
    return array


def from_behind(value, axis, steps):
    count = lax.axis_size(axis)
    initial, last = (max(0, -steps), min(count, count - steps))
    return lax.ppermute(value, axis, [(source, source + steps) for source in range(initial, last)])


def gelu_gate(value):
    inner = 0.7978845608 * (value + 0.044715 * value * value * value)
    return 0.5 * value * (1.0 + jnp.tanh(inner))


def gelu_derivative(value):
    inner = 0.7978845608 * (value + 0.044715 * value * value * value)
    tangent = jnp.tanh(inner)
    return 0.5 * (1.0 + tangent) + 0.5 * value * (1.0 - tangent * tangent) * 0.7978845608 * (
        1.0 + 0.134145 * value * value
    )


def select_position(array, position_index):
    return lax.dynamic_index_in_dim(array, position_index, 0, keepdims=False)


def local(saved_inputs, pooled_adjoint, weights):
    section_id = lax.axis_index("section")
    is_last = section_id == lax.axis_size("section") - 1
    batch_rows = saved_inputs.shape[2]
    channel_width = weights.shape[2] // 3
    dilation_amount = DILATION_STEP
    kernel_core = lax.axis_index("core")
    kernel_half = weights.shape[2] // 2
    own_columns = lax.dynamic_slice_in_dim(weights[0], kernel_core * kernel_half, kernel_half, axis=1)
    n_gx, n_gy = lax.axis_size("x"), lax.axis_size("y")
    own_columns = lax.all_gather(own_columns, "x", axis=0, tiled=False)
    own_columns = lax.all_gather(own_columns, "y", axis=1, tiled=False)
    own_columns = own_columns.reshape(n_gx * n_gy * own_columns.shape[2], kernel_half)
    partner_columns = lax.ppermute(own_columns, "core", [(0, 1), (1, 0)])
    full_kernel = jnp.where(
        kernel_core == 0,
        jnp.concatenate([own_columns, partner_columns], axis=1),
        jnp.concatenate([partner_columns, own_columns], axis=1),
    )
    seq_index = lax.axis_index(SEQ_AXES)
    sequence_length = lax.axis_size(SEQ_AXES) * batch_rows
    inputs_widened = with_halo(saved_inputs[0], ((SEQ_AXES, 1),), dilation_amount)
    upsampled = jnp.repeat(pooled_adjoint, 2, axis=1) * 0.5
    upsampled_widened = with_halo(upsampled, ((SEQ_AXES, 1),), 2 * dilation_amount)
    value_rows = inputs_widened.astype(jnp.float32)
    norm_scale = lax.rsqrt(jnp.mean(value_rows * value_rows, axis=-1, keepdims=True) + 1e-05)
    normalized_input = value_rows * norm_scale
    activation_widened = gelu_gate(normalized_input).astype(jnp.bfloat16)
    slope = gelu_derivative(normalized_input)
    wide_rows = batch_rows + 2 * dilation_amount

    def block(cotangent_widened, cotangent_state, scale, normalized, derivative, rows):
        cotangent_kernel_taps = jnp.concatenate(
            [
                cotangent_widened[
                    :,
                    (2 - kernel_offset) * dilation_amount : (2 - kernel_offset) * dilation_amount
                    + rows,
                ]
                for kernel_offset in range(3)
            ],
            axis=-1,
        )
        reverse_propagate = jnp.einsum(
            "npj,cj->npc", cotangent_kernel_taps, full_kernel, preferred_element_type=jnp.float32
        )
        derivative_gradient = reverse_propagate * derivative
        centered_average = jnp.mean(derivative_gradient * normalized, axis=-1, keepdims=True)
        return (
            cotangent_state.astype(jnp.float32)
            + scale * (derivative_gradient - normalized * centered_average)
        ).astype(jnp.bfloat16)

    upsampled_halo = upsampled_widened[:, dilation_amount : dilation_amount + wide_rows]
    upper_output = block(
        upsampled_widened, upsampled_halo, norm_scale, normalized_input, slope, wide_rows
    )
    position = seq_index * batch_rows - dilation_amount + jnp.arange(wide_rows)
    inside = (position >= 0) & (position < sequence_length)
    upper_output = jnp.where(inside[None, :, None], upper_output, jnp.zeros_like(upper_output))
    incoming = from_behind(upper_output, "section", -1)
    cotangent_widened = jnp.where(is_last, upsampled_halo, incoming)
    centre = slice(dilation_amount, dilation_amount + batch_rows)
    cotangent_state = cotangent_widened[:, centre]
    results = block(
        cotangent_widened,
        cotangent_state,
        norm_scale[:, centre],
        normalized_input[:, centre],
        slope[:, centre],
        batch_rows,
    )
    activation_kernel_taps = jnp.stack(
        [
            activation_widened[
                :, kernel_offset * dilation_amount : kernel_offset * dilation_amount + batch_rows
            ]
            for kernel_offset in range(3)
        ],
        axis=0,
    )
    grad_total = jnp.einsum(
        "knpc,npo->cko", activation_kernel_taps, cotangent_state, preferred_element_type=jnp.float32
    ).reshape(channel_width, 3 * channel_width)
    micro_batch = saved_inputs.shape[1]
    n_dp = lax.axis_size(("x", "y"))
    n_zl = lax.axis_size("zl")
    core_index = lax.axis_index("core")
    swap = [(0, 1), (1, 0)]
    owned_rows = channel_width // n_dp
    half = 3 * channel_width // 2
    own_half = lax.dynamic_slice_in_dim(grad_total, core_index * half, half, axis=1)
    other_half = lax.dynamic_slice_in_dim(grad_total, (1 - core_index) * half, half, axis=1)
    chip_half = own_half + lax.ppermute(other_half, "core", swap)
    pieces = chip_half.astype(jnp.bfloat16).reshape(n_dp, owned_rows, half)
    received = lax.all_to_all(pieces, ("x", "y"), 0, 0, tiled=True)
    owned = jnp.sum(received.astype(jnp.float32), axis=0)
    copies = jnp.broadcast_to(owned.astype(jnp.bfloat16)[None], (n_zl, owned_rows, half))
    summed = jnp.sum(lax.all_to_all(copies, "zl", 0, 0, tiled=True).astype(jnp.float32), axis=0)
    half_grad = (summed / (micro_batch * n_dp)).astype(jnp.bfloat16)
    partner_grad = lax.ppermute(half_grad, "core", swap)
    weight_grad = jnp.where(
        core_index == 0,
        jnp.concatenate([half_grad, partner_grad], axis=1),
        jnp.concatenate([partner_grad, half_grad], axis=1),
    )
    return (results[None], weight_grad[None])


def split_mesh(mesh):
    dp_devices = mesh.devices[0, :, 0]
    n_x = len({device.coords[0] for device in dp_devices})
    n_core = len({device.core_on_chip for device in mesh.devices[0, 0, :]})
    n_section, n_dp, n_seq = mesh.devices.shape
    shape = (n_section, n_x, n_dp // n_x, n_seq // n_core, n_core)
    return Mesh(mesh.devices.reshape(shape), ("section", "x", "y", "zl", "core"))


def solution(mesh):
    fine = split_mesh(mesh)
    dp, seq = ("x", "y"), SEQ_AXES
    in_specs = (P("section", dp, seq, None), P(dp, seq, None), P("section", dp, None))
    out_specs = (P("section", dp, seq, None), P("section", dp, None))
    return jax.shard_map(local, mesh=fine, in_specs=in_specs, out_specs=out_specs, check_vma=False)
```

```python
import jax
import jax.numpy as jnp
from jax import lax
from jax.sharding import Mesh, PartitionSpec as P

DILATION_STEP = 16
SEQ_AXES = ("zl", "core")


def with_halo(array, sides, width):
    for axis, dim in sides:
        count, length = (lax.axis_size(axis), array.shape[dim])
        up = [(i, (i + 1) % count) for i in range(count - 1)]
        down = [(j, i) for i, j in up]
        last = lax.slice_in_dim(array, length - width, length, axis=dim)
        initial = lax.slice_in_dim(array, 0, width, axis=dim)
        before = lax.ppermute(last, axis, up)
        after = lax.ppermute(initial, axis, down)
        array = jnp.concatenate([before, array, after], axis=dim)
    return array


def from_behind(value, axis, steps):
    count = lax.axis_size(axis)
    initial, last = (max(0, -steps), min(count, count - steps))
    return lax.ppermute(value, axis, [(source, source + steps) for source in range(initial, last)])


def gelu_gate(value):
    inner = 0.7978845608 * (value + 0.044715 * value * value * value)
    return 0.5 * value * (1.0 + jnp.tanh(inner))


def gelu_derivative(value):
    inner = 0.7978845608 * (value + 0.044715 * value * value * value)
    tangent = jnp.tanh(inner)
    return 0.5 * (1.0 + tangent) + 0.5 * value * (1.0 - tangent * tangent) * 0.7978845608 * (
        1.0 + 0.134145 * value * value
    )


def select_position(array, position_index):
    return lax.dynamic_index_in_dim(array, position_index, 0, keepdims=False)


def local(saved_inputs, pooled_adjoint, weights):
    section_id = lax.axis_index("section")
    is_last = section_id == lax.axis_size("section") - 1
    batch_rows = saved_inputs.shape[2]
    channel_width = weights.shape[2] // 3
    dilation_amount = DILATION_STEP
    kernel_core = lax.axis_index("core")
    kernel_half = weights.shape[2] // 2
    own_columns = lax.dynamic_slice_in_dim(weights[0], kernel_core * kernel_half, kernel_half, axis=1)
    n_gx, n_gy = lax.axis_size("x"), lax.axis_size("y")
    own_columns = lax.all_gather(own_columns, "x", axis=0, tiled=False)
    own_columns = lax.all_gather(own_columns, "y", axis=1, tiled=False)
    own_columns = own_columns.reshape(n_gx * n_gy * own_columns.shape[2], kernel_half)
    partner_columns = lax.ppermute(own_columns, "core", [(0, 1), (1, 0)])
    full_kernel = jnp.where(
        kernel_core == 0,
        jnp.concatenate([own_columns, partner_columns], axis=1),
        jnp.concatenate([partner_columns, own_columns], axis=1),
    )
    seq_index = lax.axis_index(SEQ_AXES)
    sequence_length = lax.axis_size(SEQ_AXES) * batch_rows
    inputs_widened = with_halo(saved_inputs[0], ((SEQ_AXES, 1),), dilation_amount)
    upsampled = jnp.repeat(pooled_adjoint, 2, axis=1) * 0.5
    upsampled_widened = with_halo(upsampled, ((SEQ_AXES, 1),), 2 * dilation_amount)
    value_rows = inputs_widened.astype(jnp.float32)
    norm_scale = lax.rsqrt(jnp.mean(value_rows * value_rows, axis=-1, keepdims=True) + 1e-05)
    normalized_input = value_rows * norm_scale
    activation_widened = gelu_gate(normalized_input).astype(jnp.bfloat16)
    slope = gelu_derivative(normalized_input)
    wide_rows = batch_rows + 2 * dilation_amount

    def block(cotangent_widened, cotangent_state, scale, normalized, derivative, rows):
        cotangent_kernel_taps = jnp.concatenate(
            [
                cotangent_widened[
                    :,
                    (2 - kernel_offset) * dilation_amount : (2 - kernel_offset) * dilation_amount
                    + rows,
                ]
                for kernel_offset in range(3)
            ],
            axis=-1,
        )
        reverse_propagate = jnp.einsum(
            "npj,cj->npc", cotangent_kernel_taps, full_kernel, preferred_element_type=jnp.float32
        )
        derivative_gradient = reverse_propagate * derivative
        centered_average = jnp.mean(derivative_gradient * normalized, axis=-1, keepdims=True)
        return (
            cotangent_state.astype(jnp.float32)
            + scale * (derivative_gradient - normalized * centered_average)
        ).astype(jnp.bfloat16)

    upsampled_halo = upsampled_widened[:, dilation_amount : dilation_amount + wide_rows]
    upper_output = block(
        upsampled_widened, upsampled_halo, norm_scale, normalized_input, slope, wide_rows
    )
    position = seq_index * batch_rows - dilation_amount + jnp.arange(wide_rows)
    inside = (position >= 0) & (position < sequence_length)
    upper_output = jnp.where(inside[None, :, None], upper_output, jnp.zeros_like(upper_output))
    incoming = from_behind(upper_output, "section", -1)
    cotangent_widened = jnp.where(is_last, upsampled_halo, incoming)
    centre = slice(dilation_amount, dilation_amount + batch_rows)
    cotangent_state = cotangent_widened[:, centre]
    results = block(
        cotangent_widened,
        cotangent_state,
        norm_scale[:, centre],
        normalized_input[:, centre],
        slope[:, centre],
        batch_rows,
    )
    activation_kernel_taps = jnp.stack(
        [
            activation_widened[
                :, kernel_offset * dilation_amount : kernel_offset * dilation_amount + batch_rows
            ]
            for kernel_offset in range(3)
        ],
        axis=0,
    )
    grad_total = jnp.einsum(
        "knpc,npo->cko", activation_kernel_taps, cotangent_state, preferred_element_type=jnp.float32
    ).reshape(channel_width, 3 * channel_width)
    micro_batch = saved_inputs.shape[1]
    n_dp = lax.axis_size(("x", "y"))
    n_zl = lax.axis_size("zl")
    core_index = lax.axis_index("core")
    swap = [(0, 1), (1, 0)]
    owned_rows = channel_width // n_dp
    half = 3 * channel_width // 2
    rounded_total = grad_total.astype(jnp.bfloat16)
    own_half = lax.dynamic_slice_in_dim(rounded_total, core_index * half, half, axis=1)
    other_half = lax.dynamic_slice_in_dim(rounded_total, (1 - core_index) * half, half, axis=1)
    chip_half = own_half.astype(jnp.float32) + lax.ppermute(other_half, "core", swap).astype(
        jnp.float32
    )
    pieces = chip_half.astype(jnp.bfloat16).reshape(n_dp, owned_rows, half)
    received = lax.all_to_all(pieces, ("x", "y"), 0, 0, tiled=True)
    owned = jnp.sum(received.astype(jnp.float32), axis=0)
    copies = jnp.broadcast_to(owned.astype(jnp.bfloat16)[None], (n_zl, owned_rows, half))
    summed = jnp.sum(lax.all_to_all(copies, "zl", 0, 0, tiled=True).astype(jnp.float32), axis=0)
    half_grad = (summed / (micro_batch * n_dp)).astype(jnp.bfloat16)
    partner_grad = lax.ppermute(half_grad, "core", swap)
    weight_grad = jnp.where(
        core_index == 0,
        jnp.concatenate([half_grad, partner_grad], axis=1),
        jnp.concatenate([partner_grad, half_grad], axis=1),
    )
    return (results[None], weight_grad[None])


def split_mesh(mesh):
    dp_devices = mesh.devices[0, :, 0]
    n_x = len({device.coords[0] for device in dp_devices})
    n_core = len({device.core_on_chip for device in mesh.devices[0, 0, :]})
    n_section, n_dp, n_seq = mesh.devices.shape
    shape = (n_section, n_x, n_dp // n_x, n_seq // n_core, n_core)
    return Mesh(mesh.devices.reshape(shape), ("section", "x", "y", "zl", "core"))


def solution(mesh):
    fine = split_mesh(mesh)
    dp, seq = ("x", "y"), SEQ_AXES
    in_specs = (P("section", dp, seq, None), P(dp, seq, None), P("section", dp, None))
    out_specs = (P("section", dp, seq, None), P("section", dp, None))
    return jax.shard_map(local, mesh=fine, in_specs=in_specs, out_specs=out_specs, check_vma=False)
```
